512 devices in a mesh: row: 32 (over x, y, core), col: 16 (over z).
Axes of the slice: x: 4, y: 4, z: 16, core: 2. Of those that a mesh axis runs over, the one named last changes fastest.
Arguments:
- panel: float32 [65536, 256], P('row', 'col'), may hold values from -210 to 210
- slab: float32 [65536, 4096], P('row', 'col'), may hold values from -6 to 6
Outputs:
- triangle: float32 [256, 256], P(None, 'col')
- projected: float32 [256, 4096], P(None, 'col')
- residual: float32 [65536, 4096], P('row', 'col')
The draws below stay inside these ranges and needn't reach their ends.
All inputs are finite; a program needn't handle non-finite values.
Results may differ from the reference program's by a relative error of at most 0.0003.
Values sent between devices are 32-bit elements; how exact they have to be, the bound alone decides.
No kernel may reach another device: no remote copies, remote signals or barrier semaphores. Data moves between devices by JAX's collectives and lax.ppermute only.
A program may use at most 64 MiB of HBM per device.

```python
import math
import jax
import jax.numpy as jnp
from jax import lax

PB = 256
ROWS = 65536
TRAIL = 4096


def draw_panel(key, part):
    key_base, key_col, key_row = jax.random.split(key, 3)
    normal_part = jnp.clip(jax.random.normal(key_base, (ROWS, PB), jnp.float32), -6.0, 6.0)
    mixed = normal_part + 0.5 * jnp.roll(normal_part, 1, axis=1) + 0.3 * jnp.roll(normal_part, 2, axis=1)
    col_scale = jnp.exp(jax.random.uniform(key_col, (1, PB), jnp.float32, 0.0, math.log(10.0)))
    row_scale = jnp.exp(jax.random.uniform(key_row, (ROWS, 1), jnp.float32, 0.0, math.log(10.0)))
    rising = jnp.exp(0.5 * math.log(3.0) * jnp.arange(ROWS, dtype=jnp.float32) / ROWS)[:, None]
    return mixed * col_scale * row_scale * rising * 0.1


def block_scale(stream_key, extent, cuts, least, top_value):
    gain = 1.0
    for dim, blocks in cuts:
        steps = jax.random.uniform(jax.random.fold_in(jax.random.fold_in(stream_key, 6), dim), (blocks,), jnp.float32, least / len(cuts), top_value / len(cuts))
        gain = gain * jnp.repeat(jnp.exp(steps), extent[dim] // blocks).reshape((-1,) + (1,) * (len(extent) - 1 - dim))
    return gain


def centred(stream_key, extent, scale, limit, cuts=(), kind=jnp.bfloat16):
    array = scale * jax.random.normal(stream_key, extent, jnp.float32)
    if cuts:
        array = array * block_scale(stream_key, extent, cuts, -0.22, 0.18)
    return jnp.clip(array, -limit, limit).astype(kind)


def setup_inputs(seed: int = 0) -> dict:
    arg_keys = jax.random.split(jax.random.key(seed), 3)
    return {
        "panel": draw_panel(jax.random.fold_in(arg_keys[2], 71), 0),
        "slab": centred(arg_keys[1], (ROWS, TRAIL), 1.0, 6.0, ((0, 32), (1, 16)), jnp.float32),
    }


def reference(panel, slab):
    highest = lax.Precision.HIGHEST
    upper_factor = jnp.linalg.qr(panel, mode='r')
    sign_row = jnp.sign(jnp.diagonal(upper_factor))
    upper_factor = upper_factor * sign_row[:, None]
    triangle = upper_factor * (1.0 / math.sqrt(ROWS))
    cross_all = jnp.dot(panel.T, slab, precision=highest)
    projected = lax.linalg.triangular_solve(upper_factor, cross_all, left_side=True, lower=False, transpose_a=True)
    coefficients = lax.linalg.triangular_solve(upper_factor, projected, left_side=True, lower=False, transpose_a=False)
    residual = slab - jnp.dot(panel, coefficients, precision=highest)
    return (triangle, projected, residual)
```

```python
import math

import jax
import jax.numpy as jnp
from jax import lax
from jax.sharding import PartitionSpec as P

contract_rows = (((0,), (0,)), ((), ()))


def row_sum(x):
    n = lax.axis_size("row")
    rows, cols = x.shape
    parts = x.reshape(n, rows // n, cols)
    mine = lax.all_to_all(parts, "row", 0, 0, tiled=False).sum(0)
    copies = jnp.broadcast_to(mine[None], (n, rows // n, cols))
    return lax.all_to_all(copies, "row", 0, 0, tiled=False).reshape(rows, cols)


def per_device(panel, slab):
    highest = lax.Precision.HIGHEST
    gathered = lax.all_gather(panel, "col", axis=1, tiled=True)
    cross_local = lax.dot_general(gathered, slab, contract_rows, precision=highest)
    gram_local = lax.dot_general(gathered, gathered, contract_rows, precision=highest)
    width = gram_local.shape[1]
    summed = row_sum(jnp.concatenate([gram_local, cross_local], axis=1))
    gram_total, totals = summed[:, :width], summed[:, width:]
    lower_factor = jnp.linalg.cholesky(gram_total)
    projected = lax.linalg.triangular_solve(
        lower_factor, totals, left_side=True, lower=True, transpose_a=False
    )
    coefficients = lax.linalg.triangular_solve(
        lower_factor, projected, left_side=True, lower=True, transpose_a=True
    )
    residual = slab - jnp.dot(gathered, coefficients, precision=highest)
    col_width = panel.shape[1]
    rows_total = gathered.shape[0] * lax.axis_size("row")
    scaled = lower_factor.T * (1.0 / math.sqrt(rows_total))
    triangle = lax.dynamic_slice_in_dim(scaled, lax.axis_index("col") * col_width, col_width, 1)
    return (triangle, projected, residual)


def solution(mesh):
    placed = (P("row", "col"), P("row", "col"))
    return jax.shard_map(
        per_device,
        mesh=mesh,
        in_specs=placed,
        out_specs=(P(None, "col"), P(None, "col"), P("row", "col")),
        check_vma=False,
    )
```

```python
import math

import jax
import jax.numpy as jnp
from jax import lax
from jax.sharding import PartitionSpec as P

contract_rows = (((0,), (0,)), ((), ()))


def row_sum(x):
    n = lax.axis_size("row")
    rows, cols = x.shape
    parts = x.reshape(n, rows // n, cols)
    mine = lax.all_to_all(parts, "row", 0, 0, tiled=False).sum(0)
    copies = jnp.broadcast_to(mine[None], (n, rows // n, cols))
    return lax.all_to_all(copies, "row", 0, 0, tiled=False).reshape(rows, cols)


def per_device(panel, slab):
    highest = lax.Precision.HIGHEST
    gathered = lax.all_gather(panel, "col", axis=1, tiled=True)
    cross_local = lax.dot_general(gathered, slab, contract_rows, precision=highest)
    gram_local = lax.dot_general(gathered, gathered, contract_rows, precision=highest)
    width = gram_local.shape[1]
    summed = row_sum(jnp.concatenate([gram_local, cross_local], axis=1))
    gram_total, totals = summed[:, :width], summed[:, width:]
    lower_factor = jnp.linalg.cholesky(gram_total)
    eye = jnp.eye(lower_factor.shape[0], dtype=lower_factor.dtype)
    lower_inverse = lax.linalg.triangular_solve(
        lower_factor, eye, left_side=True, lower=True, transpose_a=False
    )
    projected = jnp.dot(lower_inverse, totals, precision=highest)
    coefficients = lax.dot_general(lower_inverse, projected, contract_rows, precision=highest)
    residual = slab - jnp.dot(gathered, coefficients, precision=highest)
    col_width = panel.shape[1]
    rows_total = gathered.shape[0] * lax.axis_size("row")
    scaled = lower_factor.T * (1.0 / math.sqrt(rows_total))
    triangle = lax.dynamic_slice_in_dim(scaled, lax.axis_index("col") * col_width, col_width, 1)
    return (triangle, projected, residual)


def solution(mesh):
    placed = (P("row", "col"), P("row", "col"))
    return jax.shard_map(
        per_device,
        mesh=mesh,
        in_specs=placed,
        out_specs=(P(None, "col"), P(None, "col"), P("row", "col")),
        check_vma=False,
    )
```

```python
import math

import jax
import jax.numpy as jnp
from jax import lax
from jax.experimental import pallas as pl
from jax.experimental.pallas import tpu as pltpu
from jax.sharding import PartitionSpec as P

contract_rows = (((0,), (0,)), ((), ()))
HIGHEST = lax.Precision.HIGHEST


def factor_kernel(gram_ref, upper_ref, inverse_ref, work_ref):
    n = gram_ref.shape[0]
    rows = lax.broadcasted_iota(jnp.int32, (n, n), 0)
    cols = lax.broadcasted_iota(jnp.int32, (n, n), 1)
    work_ref[:, :n] = gram_ref[...]
    work_ref[:, n:] = jnp.where(rows == cols, 1.0, 0.0).astype(jnp.float32)
    lane = lax.broadcasted_iota(jnp.int32, (8, 2 * n), 1)
    sub = lax.broadcasted_iota(jnp.int32, (8, 2 * n), 0)
    sub_col = lax.broadcasted_iota(jnp.int32, (8, 1), 0)

    def block(b, carry):
        base = pl.multiple_of(b * 8, 8)
        strip = work_ref[pl.ds(base, 8), :]
        for t in range(8):
            col = jnp.sum(jnp.where(lane == base + t, strip, 0.0), axis=1, keepdims=True)
            scale = 1.0 / jnp.sqrt(col[t:t + 1, :])
            pivot = strip[t:t + 1, :] * scale
            mult = jnp.where(sub_col > t, col * scale, 0.0)
            strip = jnp.where(sub == t, pivot, strip - mult * pivot)
        work_ref[pl.ds(base, 8), :] = strip
        left = jnp.where(lane[:, :n] > base + 7, strip[:, :n], 0.0)
        update = lax.dot_general(left, strip, contract_rows,
                                 precision=HIGHEST, preferred_element_type=jnp.float32)
        work_ref[...] = work_ref[...] - update
        return carry

    lax.fori_loop(0, n // 8, block, 0)
    done = work_ref[...]
    upper_ref[...] = jnp.where(cols >= rows, done[:, :n], 0.0)
    inverse_ref[...] = jnp.where(cols <= rows, done[:, n:], 0.0)


def factor(gram):
    n = gram.shape[0]
    return pl.pallas_call(
        factor_kernel,
        out_shape=(jax.ShapeDtypeStruct((n, n), jnp.float32),) * 2,
        in_specs=[pl.BlockSpec(memory_space=pltpu.VMEM)],
        out_specs=(pl.BlockSpec(memory_space=pltpu.VMEM),) * 2,
        scratch_shapes=[pltpu.VMEM((n, 2 * n), jnp.float32)],
    )(gram)


def row_sum(x):
    n = lax.axis_size("row")
    rows, cols = x.shape
    parts = x.reshape(n, rows // n, cols)
    mine = lax.all_to_all(parts, "row", 0, 0, tiled=False).sum(0)
    copies = jnp.broadcast_to(mine[None], (n, rows // n, cols))
    return lax.all_to_all(copies, "row", 0, 0, tiled=False).reshape(rows, cols)


def per_device(panel, slab):
    highest = lax.Precision.HIGHEST
    gathered = lax.all_gather(panel, "col", axis=1, tiled=True)
    cross_local = lax.dot_general(gathered, slab, contract_rows, precision=highest)
    gram_local = lax.dot_general(gathered, gathered, contract_rows, precision=highest)
    width = gram_local.shape[1]
    summed = row_sum(jnp.concatenate([gram_local, cross_local], axis=1))
    gram_total, totals = summed[:, :width], summed[:, width:]
    upper_factor, lower_inverse = factor(gram_total)
    projected = jnp.dot(lower_inverse, totals, precision=highest)
    coefficients = lax.dot_general(lower_inverse, projected, contract_rows, precision=highest)
    residual = slab - jnp.dot(gathered, coefficients, precision=highest)
    col_width = panel.shape[1]
    rows_total = gathered.shape[0] * lax.axis_size("row")
    scaled = upper_factor * (1.0 / math.sqrt(rows_total))
    triangle = lax.dynamic_slice_in_dim(scaled, lax.axis_index("col") * col_width, col_width, 1)
    return (triangle, projected, residual)


def solution(mesh):
    placed = (P("row", "col"), P("row", "col"))
    return jax.shard_map(
        per_device,
        mesh=mesh,
        in_specs=placed,
        out_specs=(P(None, "col"), P(None, "col"), P("row", "col")),
        check_vma=False,
    )
```

```python
import math

import jax
import jax.numpy as jnp
from jax import lax
from jax.experimental import pallas as pl
from jax.experimental.pallas import tpu as pltpu
from jax.sharding import PartitionSpec as P

contract_rows = (((0,), (0,)), ((), ()))
HIGHEST = lax.Precision.HIGHEST


def factor_kernel(gram_ref, upper_ref, inverse_ref, work_ref):
    n = gram_ref.shape[0]
    rows = lax.broadcasted_iota(jnp.int32, (n, n), 0)
    cols = lax.broadcasted_iota(jnp.int32, (n, n), 1)
    work_ref[:, :n] = gram_ref[...]
    work_ref[:, n:] = jnp.where(rows == cols, 1.0, 0.0).astype(jnp.float32)
    sub_col = lax.broadcasted_iota(jnp.int32, (8, 1), 0)
    half = n // 2

    def phase(first, last, lo, hi):
        width = hi - lo
        lane = lax.broadcasted_iota(jnp.int32, (8, width), 1) + lo
        sub = lax.broadcasted_iota(jnp.int32, (8, width), 0)
        key = n - lo

        def block(b, carry):
            base = pl.multiple_of(b * 8, 8)
            strip = work_ref[pl.ds(base, 8), lo:hi]
            for t in range(8):
                col = jnp.sum(jnp.where(lane[:, :key] == base + t, strip[:, :key], 0.0),
                              axis=1, keepdims=True)
                scale = 1.0 / jnp.sqrt(col[t:t + 1, :])
                pivot = strip[t:t + 1, :] * scale
                mult = jnp.where(sub_col > t, col * scale, 0.0)
                strip = jnp.where(sub == t, pivot, strip - mult * pivot)
            work_ref[pl.ds(base, 8), lo:hi] = strip
            left = jnp.where(lane[:, :key] > base + 7, strip[:, :key], 0.0)
            update = lax.dot_general(left, strip, contract_rows,
                                     precision=HIGHEST, preferred_element_type=jnp.float32)
            work_ref[lo:n, lo:hi] = work_ref[lo:n, lo:hi] - update
            return carry

        lax.fori_loop(first, last, block, 0)

    phase(0, half // 8, 0, n + half)
    phase(half // 8, n // 8, half, 2 * n)
    done = work_ref[...]
    upper_ref[...] = jnp.where(cols >= rows, done[:, :n], 0.0)
    inverse_ref[...] = jnp.where(cols <= rows, done[:, n:], 0.0)


def factor(gram):
    n = gram.shape[0]
    return pl.pallas_call(
        factor_kernel,
        out_shape=(jax.ShapeDtypeStruct((n, n), jnp.float32),) * 2,
        in_specs=[pl.BlockSpec(memory_space=pltpu.VMEM)],
        out_specs=(pl.BlockSpec(memory_space=pltpu.VMEM),) * 2,
        scratch_shapes=[pltpu.VMEM((n, 2 * n), jnp.float32)],
    )(gram)


def row_sum(x):
    n = lax.axis_size("row")
    rows, cols = x.shape
    parts = x.reshape(n, rows // n, cols)
    mine = lax.all_to_all(parts, "row", 0, 0, tiled=False).sum(0)
    copies = jnp.broadcast_to(mine[None], (n, rows // n, cols))
    return lax.all_to_all(copies, "row", 0, 0, tiled=False).reshape(rows, cols)


def per_device(panel, slab):
    highest = lax.Precision.HIGHEST
    gathered = lax.all_gather(panel, "col", axis=1, tiled=True)
    cross_local = lax.dot_general(gathered, slab, contract_rows, precision=highest)
    gram_local = lax.dot_general(gathered, gathered, contract_rows, precision=highest)
    width = gram_local.shape[1]
    summed = row_sum(jnp.concatenate([gram_local, cross_local], axis=1))
    gram_total, totals = summed[:, :width], summed[:, width:]
    upper_factor, lower_inverse = factor(gram_total)
    projected = jnp.dot(lower_inverse, totals, precision=highest)
    coefficients = lax.dot_general(lower_inverse, projected, contract_rows, precision=highest)
    residual = slab - jnp.dot(gathered, coefficients, precision=highest)
    col_width = panel.shape[1]
    rows_total = gathered.shape[0] * lax.axis_size("row")
    scaled = upper_factor * (1.0 / math.sqrt(rows_total))
    triangle = lax.dynamic_slice_in_dim(scaled, lax.axis_index("col") * col_width, col_width, 1)
    return (triangle, projected, residual)


def solution(mesh):
    placed = (P("row", "col"), P("row", "col"))
    return jax.shard_map(
        per_device,
        mesh=mesh,
        in_specs=placed,
        out_specs=(P(None, "col"), P(None, "col"), P("row", "col")),
        check_vma=False,
    )
```

```python
import math

import jax
import jax.numpy as jnp
from jax import lax
from jax.experimental import pallas as pl
from jax.experimental.pallas import tpu as pltpu
from jax.sharding import PartitionSpec as P

contract_rows = (((0,), (0,)), ((), ()))
HIGHEST = lax.Precision.HIGHEST


def factor_kernel(gram_ref, upper_ref, inverse_ref, work_ref):
    n = gram_ref.shape[0]
    rows = lax.broadcasted_iota(jnp.int32, (n, n), 0)
    cols = lax.broadcasted_iota(jnp.int32, (n, n), 1)
    work_ref[:, :n] = gram_ref[...]
    work_ref[:, n:] = jnp.where(rows == cols, 1.0, 0.0).astype(jnp.float32)
    sub_col = lax.broadcasted_iota(jnp.int32, (8, 1), 0)
    half = n // 2

    def phase(first, last, lo, hi):
        width = hi - lo
        lane = lax.broadcasted_iota(jnp.int32, (8, width), 1) + lo
        sub = lax.broadcasted_iota(jnp.int32, (8, width), 0)
        key = n - lo

        def block(b, carry):
            base = pl.multiple_of(b * 8, 8)
            strip = work_ref[pl.ds(base, 8), lo:hi]
            for t in range(8):
                col = jnp.sum(jnp.where(lane[:, :key] == base + t, strip[:, :key], 0.0),
                              axis=1, keepdims=True)
                scale = 1.0 / jnp.sqrt(col[t:t + 1, :])
                pivot = strip[t:t + 1, :] * scale
                mult = jnp.where(sub_col > t, col * scale, 0.0)
                strip = jnp.where(sub == t, pivot, strip - mult * pivot)
            work_ref[pl.ds(base, 8), lo:hi] = strip
            left = jnp.where(lane[:, :key] > base + 7, strip[:, :key], 0.0)
            update = lax.dot_general(left, strip, contract_rows,
                                     precision=HIGHEST, preferred_element_type=jnp.float32)
            work_ref[lo:n, lo:hi] = work_ref[lo:n, lo:hi] - update
            return carry

        lax.fori_loop(first, last, block, 0)

    phase(0, half // 8, 0, n + half)
    phase(half // 8, n // 8, half, 2 * n)
    done = work_ref[...]
    upper_ref[...] = jnp.where(cols >= rows, done[:, :n], 0.0)
    inverse_ref[...] = jnp.where(cols <= rows, done[:, n:], 0.0)


def factor(gram):
    n = gram.shape[0]
    return pl.pallas_call(
        factor_kernel,
        out_shape=(jax.ShapeDtypeStruct((n, n), jnp.float32),) * 2,
        in_specs=[pl.BlockSpec(memory_space=pltpu.VMEM)],
        out_specs=(pl.BlockSpec(memory_space=pltpu.VMEM),) * 2,
        scratch_shapes=[pltpu.VMEM((n, 2 * n), jnp.float32)],
    )(gram)


def col_gather(x):
    n = lax.axis_size("col")
    ahead, behind = x, x
    got = {0: x}
    for step in range(1, n // 2 + 1):
        ahead = lax.ppermute(ahead, "col", [(i, (i + 1) % n) for i in range(n)])
        got[-step] = ahead
        if step < n // 2:
            behind = lax.ppermute(behind, "col", [(i, (i - 1) % n) for i in range(n)])
            got[step] = behind
    rotated = jnp.concatenate([got[k] for k in range(-(n // 2), n - n // 2)], axis=1)
    shift = (lax.axis_index("col") - n // 2) * x.shape[1]
    return jnp.roll(rotated, shift, axis=1)


def row_sum(x):
    n = lax.axis_size("row")
    rows, cols = x.shape
    parts = x.reshape(n, rows // n, cols)
    mine = lax.all_to_all(parts, "row", 0, 0, tiled=False).sum(0)
    copies = jnp.broadcast_to(mine[None], (n, rows // n, cols))
    return lax.all_to_all(copies, "row", 0, 0, tiled=False).reshape(rows, cols)


def per_device(panel, slab):
    highest = lax.Precision.HIGHEST
    gathered = col_gather(panel)
    cross_local = lax.dot_general(gathered, slab, contract_rows, precision=highest)
    gram_local = lax.dot_general(gathered, gathered, contract_rows, precision=highest)
    width = gram_local.shape[1]
    summed = row_sum(jnp.concatenate([gram_local, cross_local], axis=1))
    gram_total, totals = summed[:, :width], summed[:, width:]
    upper_factor, lower_inverse = factor(gram_total)
    projected = jnp.dot(lower_inverse, totals, precision=highest)
    coefficients = lax.dot_general(lower_inverse, projected, contract_rows, precision=highest)
    residual = slab - jnp.dot(gathered, coefficients, precision=highest)
    col_width = panel.shape[1]
    rows_total = gathered.shape[0] * lax.axis_size("row")
    scaled = upper_factor * (1.0 / math.sqrt(rows_total))
    triangle = lax.dynamic_slice_in_dim(scaled, lax.axis_index("col") * col_width, col_width, 1)
    return (triangle, projected, residual)


def solution(mesh):
    placed = (P("row", "col"), P("row", "col"))
    return jax.shard_map(
        per_device,
        mesh=mesh,
        in_specs=placed,
        out_specs=(P(None, "col"), P(None, "col"), P("row", "col")),
        check_vma=False,
    )
```

```python
import math

import jax
import jax.numpy as jnp
from jax import lax
from jax.experimental import pallas as pl
from jax.experimental.pallas import tpu as pltpu
from jax.sharding import PartitionSpec as P

contract_rows = (((0,), (0,)), ((), ()))
HIGHEST = lax.Precision.HIGHEST


def factor_kernel(gram_ref, upper_ref, inverse_ref, work_ref):
    n = gram_ref.shape[0]
    rows = lax.broadcasted_iota(jnp.int32, (n, n), 0)
    cols = lax.broadcasted_iota(jnp.int32, (n, n), 1)
    work_ref[:, :n] = gram_ref[...]
    work_ref[:, n:] = jnp.where(rows == cols, 1.0, 0.0).astype(jnp.float32)
    sub_col = lax.broadcasted_iota(jnp.int32, (8, 1), 0)
    half = n // 2

    def phase(first, last, lo, hi):
        width = hi - lo
        lane = lax.broadcasted_iota(jnp.int32, (8, width), 1) + lo
        sub = lax.broadcasted_iota(jnp.int32, (8, width), 0)
        key = n - lo

        def block(b, carry):
            base = pl.multiple_of(b * 8, 8)
            strip = work_ref[pl.ds(base, 8), lo:hi]
            for t in range(8):
                col = jnp.sum(jnp.where(lane[:, :key] == base + t, strip[:, :key], 0.0),
                              axis=1, keepdims=True)
                scale = 1.0 / jnp.sqrt(col[t:t + 1, :])
                pivot = strip[t:t + 1, :] * scale
                mult = jnp.where(sub_col > t, col * scale, 0.0)
                strip = jnp.where(sub == t, pivot, strip - mult * pivot)
            work_ref[pl.ds(base, 8), lo:hi] = strip
            left = jnp.where(lane[:, :key] > base + 7, strip[:, :key], 0.0)
            update = lax.dot_general(left, strip, contract_rows,
                                     precision=HIGHEST, preferred_element_type=jnp.float32)
            work_ref[lo:n, lo:hi] = work_ref[lo:n, lo:hi] - update
            return carry

        lax.fori_loop(first, last, block, 0)

    phase(0, half // 8, 0, n + half)
    phase(half // 8, n // 8, half, 2 * n)
    done = work_ref[...]
    upper_ref[...] = jnp.where(cols >= rows, done[:, :n], 0.0)
    inverse_ref[...] = jnp.where(cols <= rows, done[:, n:], 0.0)


def factor(gram):
    n = gram.shape[0]
    return pl.pallas_call(
        factor_kernel,
        out_shape=(jax.ShapeDtypeStruct((n, n), jnp.float32),) * 2,
        in_specs=[pl.BlockSpec(memory_space=pltpu.VMEM)],
        out_specs=(pl.BlockSpec(memory_space=pltpu.VMEM),) * 2,
        scratch_shapes=[pltpu.VMEM((n, 2 * n), jnp.float32)],
    )(gram)


def col_gather(x):
    n = lax.axis_size("col")
    ahead, behind = x, x
    got = {0: x}
    for step in range(1, n // 2 + 1):
        ahead = lax.ppermute(ahead, "col", [(i, (i + 1) % n) for i in range(n)])
        got[-step] = ahead
        if step < n // 2:
            behind = lax.ppermute(behind, "col", [(i, (i - 1) % n) for i in range(n)])
            got[step] = behind
    return jnp.concatenate([got[k] for k in range(-(n // 2), n - n // 2)], axis=1)


def row_sum(x):
    n = lax.axis_size("row")
    rows, cols = x.shape
    parts = x.reshape(n, rows // n, cols)
    mine = lax.all_to_all(parts, "row", 0, 0, tiled=False).sum(0)
    copies = jnp.broadcast_to(mine[None], (n, rows // n, cols))
    return lax.all_to_all(copies, "row", 0, 0, tiled=False).reshape(rows, cols)


def per_device(panel, slab):
    highest = lax.Precision.HIGHEST
    gathered = col_gather(panel)
    shift = (lax.axis_index("col") - lax.axis_size("col") // 2) * panel.shape[1]
    cross_local = lax.dot_general(gathered, slab, contract_rows, precision=highest)
    gram_local = lax.dot_general(gathered, gathered, contract_rows, precision=highest)
    width = gram_local.shape[1]
    summed = jnp.roll(row_sum(jnp.concatenate([gram_local, cross_local], axis=1)), shift, axis=0)
    gram_total, totals = jnp.roll(summed[:, :width], shift, axis=1), summed[:, width:]
    upper_factor, lower_inverse = factor(gram_total)
    projected = jnp.dot(lower_inverse, totals, precision=highest)
    coefficients = lax.dot_general(lower_inverse, projected, contract_rows, precision=highest)
    residual = slab - jnp.dot(gathered, jnp.roll(coefficients, -shift, axis=0), precision=highest)
    col_width = panel.shape[1]
    rows_total = gathered.shape[0] * lax.axis_size("row")
    scaled = upper_factor * (1.0 / math.sqrt(rows_total))
    triangle = lax.dynamic_slice_in_dim(scaled, lax.axis_index("col") * col_width, col_width, 1)
    return (triangle, projected, residual)


def solution(mesh):
    placed = (P("row", "col"), P("row", "col"))
    return jax.shard_map(
        per_device,
        mesh=mesh,
        in_specs=placed,
        out_specs=(P(None, "col"), P(None, "col"), P("row", "col")),
        check_vma=False,
    )
```

```python
import math

import jax
import jax.numpy as jnp
from jax import lax
from jax.experimental import pallas as pl
from jax.experimental.pallas import tpu as pltpu
from jax.sharding import PartitionSpec as P

contract_rows = (((0,), (0,)), ((), ()))
HIGHEST = lax.Precision.HIGHEST


def factor_kernel(gram_ref, upper_ref, inverse_ref, work_ref, left_ref):
    n = gram_ref.shape[0]
    rows = lax.broadcasted_iota(jnp.int32, (n, n), 0)
    cols = lax.broadcasted_iota(jnp.int32, (n, n), 1)
    work_ref[:, :n] = gram_ref[...]
    work_ref[:, n:] = jnp.where(rows == cols, 1.0, 0.0).astype(jnp.float32)
    sub_col = lax.broadcasted_iota(jnp.int32, (8, 1), 0)
    half = n // 2

    def phase(first, last, lo, hi):
        width = hi - lo
        lane = lax.broadcasted_iota(jnp.int32, (8, width), 1) + lo
        sub = lax.broadcasted_iota(jnp.int32, (8, width), 0)
        key = n - lo

        def block(b, strip):
            base = pl.multiple_of(b * 8, 8)
            for t in range(8):
                col = jnp.sum(jnp.where(lane[:, :key] == base + t, strip[:, :key], 0.0),
                              axis=1, keepdims=True)
                scale = 1.0 / jnp.sqrt(col[t:t + 1, :])
                pivot = strip[t:t + 1, :] * scale
                mult = jnp.where(sub_col > t, col * scale, 0.0)
                strip = jnp.where(sub == t, pivot, strip - mult * pivot)
            work_ref[pl.ds(base, 8), lo:hi] = strip
            left = jnp.where(lane[:, :key] > base + 7, strip[:, :key], 0.0)
            left_ref[lo:n, :] = jnp.transpose(left)
            after = pl.multiple_of(jnp.minimum(base + 8, n - 8), 8)
            nearest = left_ref[pl.ds(after, 8), :]
            following = work_ref[pl.ds(after, 8), lo:hi] - jnp.dot(
                nearest, strip, precision=HIGHEST, preferred_element_type=jnp.float32)
            update = jnp.dot(left_ref[lo:n, :], strip, precision=HIGHEST,
                             preferred_element_type=jnp.float32)
            work_ref[lo:n, lo:hi] = work_ref[lo:n, lo:hi] - update
            return following

        start = work_ref[first * 8:first * 8 + 8, lo:hi]
        lax.fori_loop(first, last, block, start, unroll=2)

    phase(0, half // 8, 0, n + half)
    phase(half // 8, n // 8, half, 2 * n)
    done = work_ref[...]
    upper_ref[...] = jnp.where(cols >= rows, done[:, :n], 0.0)
    inverse_ref[...] = jnp.where(cols <= rows, done[:, n:], 0.0)


def factor(gram):
    n = gram.shape[0]
    return pl.pallas_call(
        factor_kernel,
        out_shape=(jax.ShapeDtypeStruct((n, n), jnp.float32),) * 2,
        in_specs=[pl.BlockSpec(memory_space=pltpu.VMEM)],
        out_specs=(pl.BlockSpec(memory_space=pltpu.VMEM),) * 2,
        scratch_shapes=[pltpu.VMEM((n, 2 * n), jnp.float32), pltpu.VMEM((n, 8), jnp.float32)],
    )(gram)

def col_gather(x):
    n = lax.axis_size("col")
    ahead, behind = x, x
    got = {0: x}
    for step in range(1, n // 2 + 1):
        ahead = lax.ppermute(ahead, "col", [(i, (i + 1) % n) for i in range(n)])
        got[-step] = ahead
        if step < n // 2:
            behind = lax.ppermute(behind, "col", [(i, (i - 1) % n) for i in range(n)])
            got[step] = behind
    return jnp.concatenate([got[k] for k in range(-(n // 2), n - n // 2)], axis=1)


def row_sum(x):
    n = lax.axis_size("row")
    rows, cols = x.shape
    parts = x.reshape(n, rows // n, cols)
    mine = lax.all_to_all(parts, "row", 0, 0, tiled=False).sum(0)
    copies = jnp.broadcast_to(mine[None], (n, rows // n, cols))
    return lax.all_to_all(copies, "row", 0, 0, tiled=False).reshape(rows, cols)


def per_device(panel, slab):
    highest = lax.Precision.HIGHEST
    gathered = col_gather(panel)
    shift = (lax.axis_index("col") - lax.axis_size("col") // 2) * panel.shape[1]
    cross_local = lax.dot_general(gathered, slab, contract_rows, precision=highest)
    gram_local = lax.dot_general(gathered, gathered, contract_rows, precision=highest)
    width = gram_local.shape[1]
    summed = jnp.roll(row_sum(jnp.concatenate([gram_local, cross_local], axis=1)), shift, axis=0)
    gram_total, totals = jnp.roll(summed[:, :width], shift, axis=1), summed[:, width:]
    upper_factor, lower_inverse = factor(gram_total)
    projected = jnp.dot(lower_inverse, totals, precision=highest)
    coefficients = lax.dot_general(lower_inverse, projected, contract_rows, precision=highest)
    residual = slab - jnp.dot(gathered, jnp.roll(coefficients, -shift, axis=0), precision=highest)
    col_width = panel.shape[1]
    rows_total = gathered.shape[0] * lax.axis_size("row")
    scaled = upper_factor * (1.0 / math.sqrt(rows_total))
    triangle = lax.dynamic_slice_in_dim(scaled, lax.axis_index("col") * col_width, col_width, 1)
    return (triangle, projected, residual)


def solution(mesh):
    placed = (P("row", "col"), P("row", "col"))
    return jax.shard_map(
        per_device,
        mesh=mesh,
        in_specs=placed,
        out_specs=(P(None, "col"), P(None, "col"), P("row", "col")),
        check_vma=False,
    )
```

```python
import math

import jax
import jax.numpy as jnp
from jax import lax
from jax.experimental import pallas as pl
from jax.experimental.pallas import tpu as pltpu
from jax.sharding import PartitionSpec as P

contract_rows = (((0,), (0,)), ((), ()))
HIGHEST = lax.Precision.HIGHEST


def factor_kernel(gram_ref, upper_ref, inverse_ref, work_ref, left_ref):
    n = gram_ref.shape[0]
    rows = lax.broadcasted_iota(jnp.int32, (n, n), 0)
    cols = lax.broadcasted_iota(jnp.int32, (n, n), 1)
    work_ref[:, :n] = gram_ref[...]
    work_ref[:, n:] = jnp.where(rows == cols, 1.0, 0.0).astype(jnp.float32)
    sub_col = lax.broadcasted_iota(jnp.int32, (8, 1), 0)
    half = n // 2

    def phase(first, last, lo, hi):
        width = hi - lo
        lane = lax.broadcasted_iota(jnp.int32, (8, width), 1) + lo
        sub = lax.broadcasted_iota(jnp.int32, (8, width), 0)
        key = n - lo

        def block(b, strip):
            base = pl.multiple_of(b * 8, 8)
            for t in range(8):
                col = pltpu.roll(strip[:, :128], (128 - (base + t - lo)) % 128, 1)[:, 0:1]
                diag = col[t:t + 1, :]
                guess = lax.rsqrt(diag)
                scale = guess * (1.5 - 0.5 * diag * guess * guess)
                pivot = strip[t:t + 1, :] * scale
                mult = jnp.where(sub_col > t, col * scale, 0.0)
                strip = jnp.where(sub == t, pivot, strip - mult * pivot)
            work_ref[pl.ds(base, 8), lo:hi] = strip
            left = jnp.where(lane[:, :key] > base + 7, strip[:, :key], 0.0)
            left_ref[lo:n, :] = jnp.transpose(left)
            after = pl.multiple_of(jnp.minimum(base + 8, n - 8), 8)
            nearest = left_ref[pl.ds(after, 8), :]
            following = work_ref[pl.ds(after, 8), lo:hi] - jnp.dot(
                nearest, strip, precision=HIGHEST, preferred_element_type=jnp.float32)
            update = jnp.dot(left_ref[lo:n, :], strip, precision=HIGHEST,
                             preferred_element_type=jnp.float32)
            work_ref[lo:n, lo:hi] = work_ref[lo:n, lo:hi] - update
            return following

        start = work_ref[first * 8:first * 8 + 8, lo:hi]
        lax.fori_loop(first, last, block, start, unroll=2)

    phase(0, half // 8, 0, n + half)
    phase(half // 8, n // 8, half, 2 * n)
    done = work_ref[...]
    upper_ref[...] = jnp.where(cols >= rows, done[:, :n], 0.0)
    inverse_ref[...] = jnp.where(cols <= rows, done[:, n:], 0.0)


def factor(gram):
    n = gram.shape[0]
    return pl.pallas_call(
        factor_kernel,
        out_shape=(jax.ShapeDtypeStruct((n, n), jnp.float32),) * 2,
        in_specs=[pl.BlockSpec(memory_space=pltpu.VMEM)],
        out_specs=(pl.BlockSpec(memory_space=pltpu.VMEM),) * 2,
        scratch_shapes=[pltpu.VMEM((n, 2 * n), jnp.float32), pltpu.VMEM((n, 8), jnp.float32)],
    )(gram)

def col_gather(x):
    n = lax.axis_size("col")
    ahead, behind = x, x
    got = {0: x}
    for step in range(1, n // 2 + 1):
        ahead = lax.ppermute(ahead, "col", [(i, (i + 1) % n) for i in range(n)])
        got[-step] = ahead
        if step < n // 2:
            behind = lax.ppermute(behind, "col", [(i, (i - 1) % n) for i in range(n)])
            got[step] = behind
    return jnp.concatenate([got[k] for k in range(-(n // 2), n - n // 2)], axis=1)


def row_sum(x):
    n = lax.axis_size("row")
    rows, cols = x.shape
    parts = x.reshape(n, rows // n, cols)
    mine = lax.all_to_all(parts, "row", 0, 0, tiled=False).sum(0)
    copies = jnp.broadcast_to(mine[None], (n, rows // n, cols))
    return lax.all_to_all(copies, "row", 0, 0, tiled=False).reshape(rows, cols)


def per_device(panel, slab):
    highest = lax.Precision.HIGHEST
    gathered = col_gather(panel)
    shift = (lax.axis_index("col") - lax.axis_size("col") // 2) * panel.shape[1]
    cross_local = lax.dot_general(gathered, slab, contract_rows, precision=highest)
    gram_local = lax.dot_general(gathered, gathered, contract_rows, precision=highest)
    width = gram_local.shape[1]
    summed = jnp.roll(row_sum(jnp.concatenate([gram_local, cross_local], axis=1)), shift, axis=0)
    gram_total, totals = jnp.roll(summed[:, :width], shift, axis=1), summed[:, width:]
    upper_factor, lower_inverse = factor(gram_total)
    projected = jnp.dot(lower_inverse, totals, precision=highest)
    coefficients = lax.dot_general(lower_inverse, projected, contract_rows, precision=highest)
    residual = slab - jnp.dot(gathered, jnp.roll(coefficients, -shift, axis=0), precision=highest)
    col_width = panel.shape[1]
    rows_total = gathered.shape[0] * lax.axis_size("row")
    scaled = upper_factor * (1.0 / math.sqrt(rows_total))
    triangle = lax.dynamic_slice_in_dim(scaled, lax.axis_index("col") * col_width, col_width, 1)
    return (triangle, projected, residual)


def solution(mesh):
    placed = (P("row", "col"), P("row", "col"))
    return jax.shard_map(
        per_device,
        mesh=mesh,
        in_specs=placed,
        out_specs=(P(None, "col"), P(None, "col"), P("row", "col")),
        check_vma=False,
    )
```

```python
import math

import jax
import jax.numpy as jnp
from jax import lax
from jax.experimental import pallas as pl
from jax.experimental.pallas import tpu as pltpu
from jax.sharding import PartitionSpec as P

contract_rows = (((0,), (0,)), ((), ()))
HIGHEST = lax.Precision.HIGHEST


def factor_kernel(gram_ref, upper_ref, inverse_ref, work_ref, left_ref):
    n = gram_ref.shape[0]
    rows = lax.broadcasted_iota(jnp.int32, (n, n), 0)
    cols = lax.broadcasted_iota(jnp.int32, (n, n), 1)
    work_ref[:, :n] = gram_ref[...]
    work_ref[:, n:] = jnp.where(rows == cols, 1.0, 0.0).astype(jnp.float32)
    sub_col = lax.broadcasted_iota(jnp.int32, (8, 1), 0)
    half = n // 2

    def phase(first, last, lo, hi):
        width = hi - lo
        lane = lax.broadcasted_iota(jnp.int32, (8, width), 1) + lo
        sub = lax.broadcasted_iota(jnp.int32, (8, width), 0)
        key = n - lo

        def block(b, strip):
            base = pl.multiple_of(b * 8, 8)
            for t in range(8):
                col = jnp.sum(jnp.where(lane[:, :128] == base + t, strip[:, :128], 0.0),
                              axis=1, keepdims=True)
                diag = col[t:t + 1, :]
                guess = lax.rsqrt(diag)
                scale = guess * (1.5 - 0.5 * diag * guess * guess)
                pivot = strip[t:t + 1, :] * scale
                mult = jnp.where(sub_col > t, col * scale, 0.0)
                strip = jnp.where(sub == t, pivot, strip - mult * pivot)
            work_ref[pl.ds(base, 8), lo:hi] = strip
            left = jnp.where(lane[:, :key] > base + 7, strip[:, :key], 0.0)
            left_ref[lo:n, :] = jnp.transpose(left)
            after = pl.multiple_of(jnp.minimum(base + 8, n - 8), 8)
            nearest = left_ref[pl.ds(after, 8), :]
            following = work_ref[pl.ds(after, 8), lo:hi] - jnp.dot(
                nearest, strip, precision=HIGHEST, preferred_element_type=jnp.float32)
            update = jnp.dot(left_ref[lo:n, :], strip, precision=HIGHEST,
                             preferred_element_type=jnp.float32)
            work_ref[lo:n, lo:hi] = work_ref[lo:n, lo:hi] - update
            return following

        start = work_ref[first * 8:first * 8 + 8, lo:hi]
        lax.fori_loop(first, last, block, start, unroll=2)

    phase(0, half // 8, 0, n + half)
    phase(half // 8, n // 8, half, 2 * n)
    done = work_ref[...]
    upper_ref[...] = jnp.where(cols >= rows, done[:, :n], 0.0)
    inverse_ref[...] = jnp.where(cols <= rows, done[:, n:], 0.0)


def factor(gram):
    n = gram.shape[0]
    return pl.pallas_call(
        factor_kernel,
        out_shape=(jax.ShapeDtypeStruct((n, n), jnp.float32),) * 2,
        in_specs=[pl.BlockSpec(memory_space=pltpu.VMEM)],
        out_specs=(pl.BlockSpec(memory_space=pltpu.VMEM),) * 2,
        scratch_shapes=[pltpu.VMEM((n, 2 * n), jnp.float32), pltpu.VMEM((n, 8), jnp.float32)],
    )(gram)

def col_gather(x):
    n = lax.axis_size("col")
    ahead, behind = x, x
    got = {0: x}
    for step in range(1, n // 2 + 1):
        ahead = lax.ppermute(ahead, "col", [(i, (i + 1) % n) for i in range(n)])
        got[-step] = ahead
        if step < n // 2:
            behind = lax.ppermute(behind, "col", [(i, (i - 1) % n) for i in range(n)])
            got[step] = behind
    return jnp.concatenate([got[k] for k in range(-(n // 2), n - n // 2)], axis=1)


def row_sum(x):
    n = lax.axis_size("row")
    rows, cols = x.shape
    parts = x.reshape(n, rows // n, cols)
    mine = lax.all_to_all(parts, "row", 0, 0, tiled=False).sum(0)
    copies = jnp.broadcast_to(mine[None], (n, rows // n, cols))
    return lax.all_to_all(copies, "row", 0, 0, tiled=False).reshape(rows, cols)


def per_device(panel, slab):
    highest = lax.Precision.HIGHEST
    gathered = col_gather(panel)
    shift = (lax.axis_index("col") - lax.axis_size("col") // 2) * panel.shape[1]
    cross_local = lax.dot_general(gathered, slab, contract_rows, precision=highest)
    gram_local = lax.dot_general(gathered, gathered, contract_rows, precision=highest)
    width = gram_local.shape[1]
    summed = jnp.roll(row_sum(jnp.concatenate([gram_local, cross_local], axis=1)), shift, axis=0)
    gram_total, totals = jnp.roll(summed[:, :width], shift, axis=1), summed[:, width:]
    upper_factor, lower_inverse = factor(gram_total)
    projected = jnp.dot(lower_inverse, totals, precision=highest)
    coefficients = lax.dot_general(lower_inverse, projected, contract_rows, precision=highest)
    residual = slab - jnp.dot(gathered, jnp.roll(coefficients, -shift, axis=0), precision=highest)
    col_width = panel.shape[1]
    rows_total = gathered.shape[0] * lax.axis_size("row")
    scaled = upper_factor * (1.0 / math.sqrt(rows_total))
    triangle = lax.dynamic_slice_in_dim(scaled, lax.axis_index("col") * col_width, col_width, 1)
    return (triangle, projected, residual)


def solution(mesh):
    placed = (P("row", "col"), P("row", "col"))
    return jax.shard_map(
        per_device,
        mesh=mesh,
        in_specs=placed,
        out_specs=(P(None, "col"), P(None, "col"), P("row", "col")),
        check_vma=False,
    )
```

```python
import math

import jax
import jax.numpy as jnp
from jax import lax
from jax.experimental import pallas as pl
from jax.experimental.pallas import tpu as pltpu
from jax.sharding import PartitionSpec as P

contract_rows = (((0,), (0,)), ((), ()))
HIGHEST = lax.Precision.HIGHEST


def factor_kernel(gram_ref, upper_ref, inverse_ref, work_ref, left_ref):
    n = gram_ref.shape[0]
    rows = lax.broadcasted_iota(jnp.int32, (n, n), 0)
    cols = lax.broadcasted_iota(jnp.int32, (n, n), 1)
    work_ref[:, :n] = gram_ref[...]
    work_ref[:, n:] = jnp.where(rows == cols, 1.0, 0.0).astype(jnp.float32)
    sub_col = lax.broadcasted_iota(jnp.int32, (8, 1), 0)
    half = n // 2

    def phase(first, last, lo, hi):
        width = hi - lo
        lane = lax.broadcasted_iota(jnp.int32, (8, width), 1) + lo
        sub = lax.broadcasted_iota(jnp.int32, (8, width), 0)
        key = n - lo

        def block(b, strip):
            base = pl.multiple_of(b * 8, 8)
            cols = [jnp.sum(jnp.where(lane[:, :128] == base + k, strip[:, :128], 0.0),
                            axis=1, keepdims=True) for k in range(8)]
            factor_cols, inverse_diag = [], []
            for k in range(8):
                diag = cols[k][k:k + 1, :]
                guess = lax.rsqrt(diag)
                scale = guess * (1.5 - 0.5 * diag * guess * guess)
                column = jnp.where(sub_col >= k, cols[k] * scale, 0.0)
                factor_cols.append(column)
                inverse_diag.append(scale)
                for m in range(k + 1, 8):
                    cols[m] = cols[m] - column * column[m:m + 1, :]
            done_rows = []
            for k in range(8):
                row = strip[k:k + 1, :]
                for m in range(k):
                    row = row - factor_cols[m][k:k + 1, :] * done_rows[m]
                done_rows.append(row * inverse_diag[k])
            strip = done_rows[0] + jnp.zeros_like(strip)
            for k in range(1, 8):
                strip = jnp.where(sub == k, done_rows[k], strip)
            work_ref[pl.ds(base, 8), lo:hi] = strip
            left = jnp.where(lane[:, :key] > base + 7, strip[:, :key], 0.0)
            left_ref[lo:n, :] = jnp.transpose(left)
            after = pl.multiple_of(jnp.minimum(base + 8, n - 8), 8)
            nearest = left_ref[pl.ds(after, 8), :]
            following = work_ref[pl.ds(after, 8), lo:hi] - jnp.dot(
                nearest, strip, precision=HIGHEST, preferred_element_type=jnp.float32)
            update = jnp.dot(left_ref[lo:n, :], strip, precision=HIGHEST,
                             preferred_element_type=jnp.float32)
            work_ref[lo:n, lo:hi] = work_ref[lo:n, lo:hi] - update
            return following

        start = work_ref[first * 8:first * 8 + 8, lo:hi]
        lax.fori_loop(first, last, block, start, unroll=2)

    phase(0, half // 8, 0, n + half)
    phase(half // 8, n // 8, half, 2 * n)
    done = work_ref[...]
    upper_ref[...] = jnp.where(cols >= rows, done[:, :n], 0.0)
    inverse_ref[...] = jnp.where(cols <= rows, done[:, n:], 0.0)


def factor(gram):
    n = gram.shape[0]
    return pl.pallas_call(
        factor_kernel,
        out_shape=(jax.ShapeDtypeStruct((n, n), jnp.float32),) * 2,
        in_specs=[pl.BlockSpec(memory_space=pltpu.VMEM)],
        out_specs=(pl.BlockSpec(memory_space=pltpu.VMEM),) * 2,
        scratch_shapes=[pltpu.VMEM((n, 2 * n), jnp.float32), pltpu.VMEM((n, 8), jnp.float32)],
    )(gram)

def col_gather(x):
    n = lax.axis_size("col")
    ahead, behind = x, x
    got = {0: x}
    for step in range(1, n // 2 + 1):
        ahead = lax.ppermute(ahead, "col", [(i, (i + 1) % n) for i in range(n)])
        got[-step] = ahead
        if step < n // 2:
            behind = lax.ppermute(behind, "col", [(i, (i - 1) % n) for i in range(n)])
            got[step] = behind
    return jnp.concatenate([got[k] for k in range(-(n // 2), n - n // 2)], axis=1)


def row_sum(x):
    n = lax.axis_size("row")
    rows, cols = x.shape
    parts = x.reshape(n, rows // n, cols)
    mine = lax.all_to_all(parts, "row", 0, 0, tiled=False).sum(0)
    copies = jnp.broadcast_to(mine[None], (n, rows // n, cols))
    return lax.all_to_all(copies, "row", 0, 0, tiled=False).reshape(rows, cols)


def per_device(panel, slab):
    highest = lax.Precision.HIGHEST
    gathered = col_gather(panel)
    shift = (lax.axis_index("col") - lax.axis_size("col") // 2) * panel.shape[1]
    cross_local = lax.dot_general(gathered, slab, contract_rows, precision=highest)
    gram_local = lax.dot_general(gathered, gathered, contract_rows, precision=highest)
    width = gram_local.shape[1]
    summed = jnp.roll(row_sum(jnp.concatenate([gram_local, cross_local], axis=1)), shift, axis=0)
    gram_total, totals = jnp.roll(summed[:, :width], shift, axis=1), summed[:, width:]
    upper_factor, lower_inverse = factor(gram_total)
    projected = jnp.dot(lower_inverse, totals, precision=highest)
    coefficients = lax.dot_general(lower_inverse, projected, contract_rows, precision=highest)
    residual = slab - jnp.dot(gathered, jnp.roll(coefficients, -shift, axis=0), precision=highest)
    col_width = panel.shape[1]
    rows_total = gathered.shape[0] * lax.axis_size("row")
    scaled = upper_factor * (1.0 / math.sqrt(rows_total))
    triangle = lax.dynamic_slice_in_dim(scaled, lax.axis_index("col") * col_width, col_width, 1)
    return (triangle, projected, residual)


def solution(mesh):
    placed = (P("row", "col"), P("row", "col"))
    return jax.shard_map(
        per_device,
        mesh=mesh,
        in_specs=placed,
        out_specs=(P(None, "col"), P(None, "col"), P("row", "col")),
        check_vma=False,
    )
```

```python
import math

import jax
import jax.numpy as jnp
from jax import lax
from jax.experimental import pallas as pl
from jax.experimental.pallas import tpu as pltpu
from jax.sharding import PartitionSpec as P

contract_rows = (((0,), (0,)), ((), ()))
HIGHEST = lax.Precision.HIGHEST


def factor_kernel(gram_ref, upper_ref, inverse_ref, work_ref, left_ref):
    n = gram_ref.shape[0]
    rows = lax.broadcasted_iota(jnp.int32, (n, n), 0)
    cols = lax.broadcasted_iota(jnp.int32, (n, n), 1)
    work_ref[:, :n] = gram_ref[...]
    work_ref[:, n:] = jnp.where(rows == cols, 1.0, 0.0).astype(jnp.float32)
    depth = 16
    sub_col = lax.broadcasted_iota(jnp.int32, (depth, 1), 0)
    half = n // 2

    def phase(first, last, lo, hi):
        width = hi - lo
        lane = lax.broadcasted_iota(jnp.int32, (depth, width), 1) + lo
        sub = lax.broadcasted_iota(jnp.int32, (depth, width), 0)
        key = n - lo

        def block(b, strip):
            base = pl.multiple_of(b * depth, depth)
            cols = [jnp.sum(jnp.where(lane[:, :128] == base + k, strip[:, :128], 0.0),
                            axis=1, keepdims=True) for k in range(depth)]
            factor_cols, inverse_diag = [], []
            for k in range(depth):
                diag = cols[k][k:k + 1, :]
                guess = lax.rsqrt(diag)
                scale = guess * (1.5 - 0.5 * diag * guess * guess)
                column = jnp.where(sub_col >= k, cols[k] * scale, 0.0)
                factor_cols.append(column)
                inverse_diag.append(scale)
                for m in range(k + 1, depth):
                    cols[m] = cols[m] - column * column[m:m + 1, :]
            done_rows = []
            for k in range(depth):
                row = strip[k:k + 1, :]
                for m in range(k):
                    row = row - factor_cols[m][k:k + 1, :] * done_rows[m]
                done_rows.append(row * inverse_diag[k])
            strip = done_rows[0] + jnp.zeros_like(strip)
            for k in range(1, depth):
                strip = jnp.where(sub == k, done_rows[k], strip)
            work_ref[pl.ds(base, depth), lo:hi] = strip
            left = jnp.where(lane[:, :key] > base + depth - 1, strip[:, :key], 0.0)
            left_ref[lo:n, :] = jnp.transpose(left)
            after = pl.multiple_of(jnp.minimum(base + depth, n - depth), depth)
            nearest = left_ref[pl.ds(after, depth), :]
            following = work_ref[pl.ds(after, depth), lo:hi] - jnp.dot(
                nearest, strip, precision=HIGHEST, preferred_element_type=jnp.float32)
            update = jnp.dot(left_ref[lo:n, :], strip, precision=HIGHEST,
                             preferred_element_type=jnp.float32)
            work_ref[lo:n, lo:hi] = work_ref[lo:n, lo:hi] - update
            return following

        start = work_ref[first * depth:(first + 1) * depth, lo:hi]
        lax.fori_loop(first, last, block, start, unroll=2)

    phase(0, half // depth, 0, n + half)
    phase(half // depth, n // depth, half, 2 * n)
    done = work_ref[...]
    upper_ref[...] = jnp.where(cols >= rows, done[:, :n], 0.0)
    inverse_ref[...] = jnp.where(cols <= rows, done[:, n:], 0.0)


def factor(gram):
    n = gram.shape[0]
    return pl.pallas_call(
        factor_kernel,
        out_shape=(jax.ShapeDtypeStruct((n, n), jnp.float32),) * 2,
        in_specs=[pl.BlockSpec(memory_space=pltpu.VMEM)],
        out_specs=(pl.BlockSpec(memory_space=pltpu.VMEM),) * 2,
        scratch_shapes=[pltpu.VMEM((n, 2 * n), jnp.float32), pltpu.VMEM((n, 16), jnp.float32)],
    )(gram)

def col_gather(x):
    n = lax.axis_size("col")
    ahead, behind = x, x
    got = {0: x}
    for step in range(1, n // 2 + 1):
        ahead = lax.ppermute(ahead, "col", [(i, (i + 1) % n) for i in range(n)])
        got[-step] = ahead
        if step < n // 2:
            behind = lax.ppermute(behind, "col", [(i, (i - 1) % n) for i in range(n)])
            got[step] = behind
    return jnp.concatenate([got[k] for k in range(-(n // 2), n - n // 2)], axis=1)


def row_sum(x):
    n = lax.axis_size("row")
    rows, cols = x.shape
    parts = x.reshape(n, rows // n, cols)
    mine = lax.all_to_all(parts, "row", 0, 0, tiled=False).sum(0)
    copies = jnp.broadcast_to(mine[None], (n, rows // n, cols))
    return lax.all_to_all(copies, "row", 0, 0, tiled=False).reshape(rows, cols)


def per_device(panel, slab):
    highest = lax.Precision.HIGHEST
    gathered = col_gather(panel)
    shift = (lax.axis_index("col") - lax.axis_size("col") // 2) * panel.shape[1]
    cross_local = lax.dot_general(gathered, slab, contract_rows, precision=highest)
    gram_local = lax.dot_general(gathered, gathered, contract_rows, precision=highest)
    width = gram_local.shape[1]
    summed = jnp.roll(row_sum(jnp.concatenate([gram_local, cross_local], axis=1)), shift, axis=0)
    gram_total, totals = jnp.roll(summed[:, :width], shift, axis=1), summed[:, width:]
    upper_factor, lower_inverse = factor(gram_total)
    projected = jnp.dot(lower_inverse, totals, precision=highest)
    coefficients = lax.dot_general(lower_inverse, projected, contract_rows, precision=highest)
    residual = slab - jnp.dot(gathered, jnp.roll(coefficients, -shift, axis=0), precision=highest)
    col_width = panel.shape[1]
    rows_total = gathered.shape[0] * lax.axis_size("row")
    scaled = upper_factor * (1.0 / math.sqrt(rows_total))
    triangle = lax.dynamic_slice_in_dim(scaled, lax.axis_index("col") * col_width, col_width, 1)
    return (triangle, projected, residual)


def solution(mesh):
    placed = (P("row", "col"), P("row", "col"))
    return jax.shard_map(
        per_device,
        mesh=mesh,
        in_specs=placed,
        out_specs=(P(None, "col"), P(None, "col"), P("row", "col")),
        check_vma=False,
    )
```

```python
import math

import jax
import jax.numpy as jnp
from jax import lax
from jax.experimental import pallas as pl
from jax.experimental.pallas import tpu as pltpu
from jax.sharding import PartitionSpec as P

contract_rows = (((0,), (0,)), ((), ()))
HIGHEST = lax.Precision.HIGHEST


def factor_kernel(gram_ref, upper_ref, inverse_ref, work_ref, left_ref):
    n = gram_ref.shape[0]
    rows = lax.broadcasted_iota(jnp.int32, (n, n), 0)
    cols = lax.broadcasted_iota(jnp.int32, (n, n), 1)
    work_ref[:, :n] = gram_ref[...]
    work_ref[:, n:] = jnp.where(rows == cols, 1.0, 0.0).astype(jnp.float32)
    depth = 32
    sub_col = lax.broadcasted_iota(jnp.int32, (depth, 1), 0)
    half = n // 2

    def phase(first, last, lo, hi):
        width = hi - lo
        lane = lax.broadcasted_iota(jnp.int32, (depth, width), 1) + lo
        sub = lax.broadcasted_iota(jnp.int32, (depth, width), 0)
        key = n - lo

        def block(b, strip):
            base = pl.multiple_of(b * depth, depth)
            cols = [jnp.sum(jnp.where(lane[:, :128] == base + k, strip[:, :128], 0.0),
                            axis=1, keepdims=True) for k in range(depth)]
            factor_cols, inverse_diag = [], []
            for k in range(depth):
                diag = cols[k][k:k + 1, :]
                guess = lax.rsqrt(diag)
                scale = guess * (1.5 - 0.5 * diag * guess * guess)
                column = jnp.where(sub_col >= k, cols[k] * scale, 0.0)
                factor_cols.append(column)
                inverse_diag.append(scale)
                for m in range(k + 1, depth):
                    cols[m] = cols[m] - column * column[m:m + 1, :]
            done_rows = []
            for k in range(depth):
                row = strip[k:k + 1, :]
                for m in range(k):
                    row = row - factor_cols[m][k:k + 1, :] * done_rows[m]
                done_rows.append(row * inverse_diag[k])
            strip = done_rows[0] + jnp.zeros_like(strip)
            for k in range(1, depth):
                strip = jnp.where(sub == k, done_rows[k], strip)
            work_ref[pl.ds(base, depth), lo:hi] = strip
            left = jnp.where(lane[:, :key] > base + depth - 1, strip[:, :key], 0.0)
            left_ref[lo:n, :] = jnp.transpose(left)
            after = pl.multiple_of(jnp.minimum(base + depth, n - depth), depth)
            nearest = left_ref[pl.ds(after, depth), :]
            following = work_ref[pl.ds(after, depth), lo:hi] - jnp.dot(
                nearest, strip, precision=HIGHEST, preferred_element_type=jnp.float32)
            update = jnp.dot(left_ref[lo:n, :], strip, precision=HIGHEST,
                             preferred_element_type=jnp.float32)
            work_ref[lo:n, lo:hi] = work_ref[lo:n, lo:hi] - update
            return following

        start = work_ref[first * depth:(first + 1) * depth, lo:hi]
        lax.fori_loop(first, last, block, start, unroll=2)

    phase(0, half // depth, 0, n + half)
    phase(half // depth, n // depth, half, 2 * n)
    done = work_ref[...]
    upper_ref[...] = jnp.where(cols >= rows, done[:, :n], 0.0)
    inverse_ref[...] = jnp.where(cols <= rows, done[:, n:], 0.0)


def factor(gram):
    n = gram.shape[0]
    return pl.pallas_call(
        factor_kernel,
        out_shape=(jax.ShapeDtypeStruct((n, n), jnp.float32),) * 2,
        in_specs=[pl.BlockSpec(memory_space=pltpu.VMEM)],
        out_specs=(pl.BlockSpec(memory_space=pltpu.VMEM),) * 2,
        scratch_shapes=[pltpu.VMEM((n, 2 * n), jnp.float32), pltpu.VMEM((n, 32), jnp.float32)],
    )(gram)

def col_gather(x):
    n = lax.axis_size("col")
    ahead, behind = x, x
    got = {0: x}
    for step in range(1, n // 2 + 1):
        ahead = lax.ppermute(ahead, "col", [(i, (i + 1) % n) for i in range(n)])
        got[-step] = ahead
        if step < n // 2:
            behind = lax.ppermute(behind, "col", [(i, (i - 1) % n) for i in range(n)])
            got[step] = behind
    return jnp.concatenate([got[k] for k in range(-(n // 2), n - n // 2)], axis=1)


def row_sum(x):
    n = lax.axis_size("row")
    rows, cols = x.shape
    parts = x.reshape(n, rows // n, cols)
    mine = lax.all_to_all(parts, "row", 0, 0, tiled=False).sum(0)
    copies = jnp.broadcast_to(mine[None], (n, rows // n, cols))
    return lax.all_to_all(copies, "row", 0, 0, tiled=False).reshape(rows, cols)


def per_device(panel, slab):
    highest = lax.Precision.HIGHEST
    gathered = col_gather(panel)
    shift = (lax.axis_index("col") - lax.axis_size("col") // 2) * panel.shape[1]
    cross_local = lax.dot_general(gathered, slab, contract_rows, precision=highest)
    gram_local = lax.dot_general(gathered, gathered, contract_rows, precision=highest)
    width = gram_local.shape[1]
    summed = jnp.roll(row_sum(jnp.concatenate([gram_local, cross_local], axis=1)), shift, axis=0)
    gram_total, totals = jnp.roll(summed[:, :width], shift, axis=1), summed[:, width:]
    upper_factor, lower_inverse = factor(gram_total)
    projected = jnp.dot(lower_inverse, totals, precision=highest)
    coefficients = lax.dot_general(lower_inverse, projected, contract_rows, precision=highest)
    residual = slab - jnp.dot(gathered, jnp.roll(coefficients, -shift, axis=0), precision=highest)
    col_width = panel.shape[1]
    rows_total = gathered.shape[0] * lax.axis_size("row")
    scaled = upper_factor * (1.0 / math.sqrt(rows_total))
    triangle = lax.dynamic_slice_in_dim(scaled, lax.axis_index("col") * col_width, col_width, 1)
    return (triangle, projected, residual)


def solution(mesh):
    placed = (P("row", "col"), P("row", "col"))
    return jax.shard_map(
        per_device,
        mesh=mesh,
        in_specs=placed,
        out_specs=(P(None, "col"), P(None, "col"), P("row", "col")),
        check_vma=False,
    )
```

```python
import math

import jax
import jax.numpy as jnp
from jax import lax
from jax.experimental import pallas as pl
from jax.experimental.pallas import tpu as pltpu
from jax.sharding import PartitionSpec as P

contract_rows = (((0,), (0,)), ((), ()))
HIGHEST = lax.Precision.HIGHEST


def factor_kernel(gram_ref, upper_ref, inverse_ref, work_ref, left_ref):
    n = gram_ref.shape[0]
    rows = lax.broadcasted_iota(jnp.int32, (n, n), 0)
    cols = lax.broadcasted_iota(jnp.int32, (n, n), 1)
    work_ref[:, :n] = gram_ref[...]
    work_ref[:, n:] = jnp.where(rows == cols, 1.0, 0.0).astype(jnp.float32)
    depth = 16
    sub_col = lax.broadcasted_iota(jnp.int32, (depth, 1), 0)
    half = n // 2

    def phase(first, last, lo, hi):
        width = hi - lo
        lane = lax.broadcasted_iota(jnp.int32, (depth, width), 1) + lo
        sub = lax.broadcasted_iota(jnp.int32, (depth, width), 0)
        key = n - lo

        def block(b, strip):
            base = pl.multiple_of(b * depth, depth)
            cols = [jnp.sum(jnp.where(lane[:, :128] == base + k, strip[:, :128], 0.0),
                            axis=1, keepdims=True) for k in range(depth)]
            factor_cols, inverse_diag = [], []
            for k in range(depth):
                diag = cols[k][k:k + 1, :]
                guess = lax.rsqrt(diag)
                scale = guess * (1.5 - 0.5 * diag * guess * guess)
                column = jnp.where(sub_col >= k, cols[k] * scale, 0.0)
                factor_cols.append(column)
                inverse_diag.append(scale)
                for m in range(k + 1, depth):
                    cols[m] = cols[m] - column * column[m:m + 1, :]
            done_rows = []
            for k in range(depth):
                row = strip[k:k + 1, :]
                for m in range(k):
                    row = row - factor_cols[m][k:k + 1, :] * done_rows[m]
                done_rows.append(row * inverse_diag[k])
            strip = done_rows[0] + jnp.zeros_like(strip)
            for k in range(1, depth):
                strip = jnp.where(sub == k, done_rows[k], strip)
            work_ref[pl.ds(base, depth), lo:hi] = strip
            left = jnp.where(lane[:, :key] > base + depth - 1, strip[:, :key], 0.0)
            left_ref[lo:n, :] = jnp.transpose(left)
            after = pl.multiple_of(jnp.minimum(base + depth, n - depth), depth)
            nearest = left_ref[pl.ds(after, depth), :]
            following = work_ref[pl.ds(after, depth), lo:hi] - jnp.dot(
                nearest, strip, precision=HIGHEST, preferred_element_type=jnp.float32)
            update = jnp.dot(left_ref[lo:n, :], strip, precision=HIGHEST,
                             preferred_element_type=jnp.float32)
            work_ref[lo:n, lo:hi] = work_ref[lo:n, lo:hi] - update
            return following

        start = work_ref[first * depth:(first + 1) * depth, lo:hi]
        lax.fori_loop(first, last, block, start, unroll=2)

    phase(0, half // depth, 0, n + half)
    phase(half // depth, n // depth, half, 2 * n)
    done = work_ref[...]
    upper_ref[...] = jnp.where(cols >= rows, done[:, :n], 0.0)
    inverse_ref[...] = jnp.where(cols <= rows, done[:, n:], 0.0)


def factor(gram):
    n = gram.shape[0]
    return pl.pallas_call(
        factor_kernel,
        out_shape=(jax.ShapeDtypeStruct((n, n), jnp.float32),) * 2,
        in_specs=[pl.BlockSpec(memory_space=pltpu.VMEM)],
        out_specs=(pl.BlockSpec(memory_space=pltpu.VMEM),) * 2,
        scratch_shapes=[pltpu.VMEM((n, 2 * n), jnp.float32), pltpu.VMEM((n, 16), jnp.float32)],
    )(gram)

def col_gather(x):
    n = lax.axis_size("col")
    ahead, behind = x, x
    got = {0: x}
    for step in range(1, n // 2 + 1):
        ahead = lax.ppermute(ahead, "col", [(i, (i + 1) % n) for i in range(n)])
        got[-step] = ahead
        if step < n // 2:
            behind = lax.ppermute(behind, "col", [(i, (i - 1) % n) for i in range(n)])
            got[step] = behind
    return jnp.concatenate([got[k] for k in range(-(n // 2), n - n // 2)], axis=1)


def row_sum(x, width):
    n = lax.axis_size("row")
    rows, cols = x.shape
    parts = x.reshape(n, rows // n, cols)
    mine = lax.all_to_all(parts, "row", 0, 0, tiled=False).sum(0)

    def spread(piece):
        copies = jnp.broadcast_to(piece[None], (n,) + piece.shape)
        return lax.all_to_all(copies, "row", 0, 0, tiled=False).reshape(rows, piece.shape[1])

    return spread(mine[:, :width]), spread(mine[:, width:])


def per_device(panel, slab):
    highest = lax.Precision.HIGHEST
    gathered = col_gather(panel)
    shift = (lax.axis_index("col") - lax.axis_size("col") // 2) * panel.shape[1]
    cross_local = lax.dot_general(gathered, slab, contract_rows, precision=highest)
    gram_local = lax.dot_general(gathered, gathered, contract_rows, precision=highest)
    width = gram_local.shape[1]
    gram_rotated, cross_rotated = row_sum(jnp.concatenate([gram_local, cross_local], axis=1), width)
    gram_total = jnp.roll(jnp.roll(gram_rotated, shift, axis=0), shift, axis=1)
    totals = jnp.roll(cross_rotated, shift, axis=0)
    upper_factor, lower_inverse = factor(gram_total)
    projected = jnp.dot(lower_inverse, totals, precision=highest)
    coefficients = lax.dot_general(lower_inverse, projected, contract_rows, precision=highest)
    residual = slab - jnp.dot(gathered, jnp.roll(coefficients, -shift, axis=0), precision=highest)
    col_width = panel.shape[1]
    rows_total = gathered.shape[0] * lax.axis_size("row")
    scaled = upper_factor * (1.0 / math.sqrt(rows_total))
    triangle = lax.dynamic_slice_in_dim(scaled, lax.axis_index("col") * col_width, col_width, 1)
    return (triangle, projected, residual)


def solution(mesh):
    placed = (P("row", "col"), P("row", "col"))
    return jax.shard_map(
        per_device,
        mesh=mesh,
        in_specs=placed,
        out_specs=(P(None, "col"), P(None, "col"), P("row", "col")),
        check_vma=False,
    )
```

```python
import math

import jax
import jax.numpy as jnp
from jax import lax
from jax.experimental import pallas as pl
from jax.experimental.pallas import tpu as pltpu
from jax.sharding import PartitionSpec as P

contract_rows = (((0,), (0,)), ((), ()))
HIGHEST = lax.Precision.HIGHEST


def factor_kernel(gram_ref, upper_ref, inverse_ref, work_ref, left_ref):
    n = gram_ref.shape[0]
    rows = lax.broadcasted_iota(jnp.int32, (n, n), 0)
    cols = lax.broadcasted_iota(jnp.int32, (n, n), 1)
    work_ref[:, :n] = gram_ref[...]
    work_ref[:, n:] = jnp.where(rows == cols, 1.0, 0.0).astype(jnp.float32)
    depth = 16
    sub_col = lax.broadcasted_iota(jnp.int32, (depth, 1), 0)
    half = n // 2

    def phase(first, last, lo, hi):
        width = hi - lo
        lane = lax.broadcasted_iota(jnp.int32, (depth, width), 1) + lo
        sub = lax.broadcasted_iota(jnp.int32, (depth, width), 0)
        key = n - lo

        def block(b, strip):
            base = pl.multiple_of(b * depth, depth)
            cols = [jnp.sum(jnp.where(lane[:, :128] == base + k, strip[:, :128], 0.0),
                            axis=1, keepdims=True) for k in range(depth)]
            factor_cols, inverse_diag = [], []
            for k in range(depth):
                diag = cols[k][k:k + 1, :]
                guess = lax.rsqrt(diag)
                scale = guess * (1.5 - 0.5 * diag * guess * guess)
                column = jnp.where(sub_col >= k, cols[k] * scale, 0.0)
                factor_cols.append(column)
                inverse_diag.append(scale)
                for m in range(k + 1, depth):
                    cols[m] = cols[m] - column * column[m:m + 1, :]
            done_rows = []
            for k in range(depth):
                row = strip[k:k + 1, :]
                for m in range(k):
                    row = row - factor_cols[m][k:k + 1, :] * done_rows[m]
                done_rows.append(row * inverse_diag[k])
            strip = done_rows[0] + jnp.zeros_like(strip)
            for k in range(1, depth):
                strip = jnp.where(sub == k, done_rows[k], strip)
            work_ref[pl.ds(base, depth), lo:hi] = strip
            left = jnp.where(lane[:, :key] > base + depth - 1, strip[:, :key], 0.0)
            left_ref[lo:n, :] = jnp.transpose(left)
            after = pl.multiple_of(jnp.minimum(base + depth, n - depth), depth)
            nearest = left_ref[pl.ds(after, depth), :]
            following = work_ref[pl.ds(after, depth), lo:hi] - jnp.dot(
                nearest, strip, precision=HIGHEST, preferred_element_type=jnp.float32)
            update = jnp.dot(left_ref[lo:n, :], strip, precision=HIGHEST,
                             preferred_element_type=jnp.float32)
            work_ref[lo:n, lo:hi] = work_ref[lo:n, lo:hi] - update
            return following

        start = work_ref[first * depth:(first + 1) * depth, lo:hi]
        lax.fori_loop(first, last, block, start, unroll=True)

    phase(0, half // depth, 0, n + half)
    phase(half // depth, n // depth, half, 2 * n)
    done = work_ref[...]
    upper_ref[...] = jnp.where(cols >= rows, done[:, :n], 0.0)
    inverse_ref[...] = jnp.where(cols <= rows, done[:, n:], 0.0)


def factor(gram):
    n = gram.shape[0]
    return pl.pallas_call(
        factor_kernel,
        out_shape=(jax.ShapeDtypeStruct((n, n), jnp.float32),) * 2,
        in_specs=[pl.BlockSpec(memory_space=pltpu.VMEM)],
        out_specs=(pl.BlockSpec(memory_space=pltpu.VMEM),) * 2,
        scratch_shapes=[pltpu.VMEM((n, 2 * n), jnp.float32), pltpu.VMEM((n, 16), jnp.float32)],
    )(gram)

def col_gather(x):
    n = lax.axis_size("col")
    ahead, behind = x, x
    got = {0: x}
    for step in range(1, n // 2 + 1):
        ahead = lax.ppermute(ahead, "col", [(i, (i + 1) % n) for i in range(n)])
        got[-step] = ahead
        if step < n // 2:
            behind = lax.ppermute(behind, "col", [(i, (i - 1) % n) for i in range(n)])
            got[step] = behind
    return jnp.concatenate([got[k] for k in range(-(n // 2), n - n // 2)], axis=1)


def row_sum(x):
    n = lax.axis_size("row")
    rows, cols = x.shape
    parts = x.reshape(n, rows // n, cols)
    mine = lax.all_to_all(parts, "row", 0, 0, tiled=False).sum(0)
    copies = jnp.broadcast_to(mine[None], (n, rows // n, cols))
    return lax.all_to_all(copies, "row", 0, 0, tiled=False).reshape(rows, cols)


def per_device(panel, slab):
    highest = lax.Precision.HIGHEST
    gathered = col_gather(panel)
    shift = (lax.axis_index("col") - lax.axis_size("col") // 2) * panel.shape[1]
    cross_local = lax.dot_general(gathered, slab, contract_rows, precision=highest)
    gram_local = lax.dot_general(gathered, gathered, contract_rows, precision=highest)
    width = gram_local.shape[1]
    summed = jnp.roll(row_sum(jnp.concatenate([gram_local, cross_local], axis=1)), shift, axis=0)
    gram_total, totals = jnp.roll(summed[:, :width], shift, axis=1), summed[:, width:]
    upper_factor, lower_inverse = factor(gram_total)
    projected = jnp.dot(lower_inverse, totals, precision=highest)
    coefficients = lax.dot_general(lower_inverse, projected, contract_rows, precision=highest)
    residual = slab - jnp.dot(gathered, jnp.roll(coefficients, -shift, axis=0), precision=highest)
    col_width = panel.shape[1]
    rows_total = gathered.shape[0] * lax.axis_size("row")
    scaled = upper_factor * (1.0 / math.sqrt(rows_total))
    triangle = lax.dynamic_slice_in_dim(scaled, lax.axis_index("col") * col_width, col_width, 1)
    return (triangle, projected, residual)


def solution(mesh):
    placed = (P("row", "col"), P("row", "col"))
    return jax.shard_map(
        per_device,
        mesh=mesh,
        in_specs=placed,
        out_specs=(P(None, "col"), P(None, "col"), P("row", "col")),
        check_vma=False,
    )
```

```python
import math

import jax
import jax.numpy as jnp
from jax import lax
from jax.experimental import pallas as pl
from jax.experimental.pallas import tpu as pltpu
from jax.sharding import PartitionSpec as P

contract_rows = (((0,), (0,)), ((), ()))
HIGHEST = lax.Precision.HIGHEST


def factor_kernel(gram_ref, upper_ref, inverse_ref, work_ref, left_ref):
    n = gram_ref.shape[0]
    rows = lax.broadcasted_iota(jnp.int32, (n, n), 0)
    cols = lax.broadcasted_iota(jnp.int32, (n, n), 1)
    work_ref[:, :n] = gram_ref[...]
    work_ref[:, n:] = jnp.where(rows == cols, 1.0, 0.0).astype(jnp.float32)
    depth = 32
    sub_col = lax.broadcasted_iota(jnp.int32, (depth, 1), 0)
    half = n // 2

    def phase(first, last, lo, hi):
        width = hi - lo
        lane = lax.broadcasted_iota(jnp.int32, (depth, width), 1) + lo
        sub = lax.broadcasted_iota(jnp.int32, (depth, width), 0)
        key = n - lo

        def block(b, strip):
            base = pl.multiple_of(b * depth, depth)
            cols = [jnp.sum(jnp.where(lane[:, :128] == base + k, strip[:, :128], 0.0),
                            axis=1, keepdims=True) for k in range(depth)]
            factor_cols, inverse_diag = [], []
            for k in range(depth):
                diag = cols[k][k:k + 1, :]
                guess = lax.rsqrt(diag)
                scale = guess * (1.5 - 0.5 * diag * guess * guess)
                column = jnp.where(sub_col >= k, cols[k] * scale, 0.0)
                factor_cols.append(column)
                inverse_diag.append(scale)
                for m in range(k + 1, depth):
                    cols[m] = cols[m] - column * column[m:m + 1, :]
            done_rows = []
            for k in range(depth):
                row = strip[k:k + 1, :]
                for m in range(k):
                    row = row - factor_cols[m][k:k + 1, :] * done_rows[m]
                done_rows.append(row * inverse_diag[k])
            strip = done_rows[0] + jnp.zeros_like(strip)
            for k in range(1, depth):
                strip = jnp.where(sub == k, done_rows[k], strip)
            work_ref[pl.ds(base, depth), lo:hi] = strip
            left = jnp.where(lane[:, :key] > base + depth - 1, strip[:, :key], 0.0)
            left_ref[lo:n, :] = jnp.transpose(left)
            after = pl.multiple_of(jnp.minimum(base + depth, n - depth), depth)
            nearest = left_ref[pl.ds(after, depth), :]
            following = work_ref[pl.ds(after, depth), lo:hi] - jnp.dot(
                nearest, strip, precision=HIGHEST, preferred_element_type=jnp.float32)
            update = jnp.dot(left_ref[lo:n, :], strip, precision=HIGHEST,
                             preferred_element_type=jnp.float32)
            work_ref[lo:n, lo:hi] = work_ref[lo:n, lo:hi] - update
            return following

        start = work_ref[first * depth:(first + 1) * depth, lo:hi]
        lax.fori_loop(first, last, block, start, unroll=True)

    phase(0, half // depth, 0, n + half)
    phase(half // depth, n // depth, half, 2 * n)
    done = work_ref[...]
    upper_ref[...] = jnp.where(cols >= rows, done[:, :n], 0.0)
    inverse_ref[...] = jnp.where(cols <= rows, done[:, n:], 0.0)


def factor(gram):
    n = gram.shape[0]
    return pl.pallas_call(
        factor_kernel,
        out_shape=(jax.ShapeDtypeStruct((n, n), jnp.float32),) * 2,
        in_specs=[pl.BlockSpec(memory_space=pltpu.VMEM)],
        out_specs=(pl.BlockSpec(memory_space=pltpu.VMEM),) * 2,
        scratch_shapes=[pltpu.VMEM((n, 2 * n), jnp.float32), pltpu.VMEM((n, 32), jnp.float32)],
    )(gram)

def col_gather(x):
    n = lax.axis_size("col")
    ahead, behind = x, x
    got = {0: x}
    for step in range(1, n // 2 + 1):
        ahead = lax.ppermute(ahead, "col", [(i, (i + 1) % n) for i in range(n)])
        got[-step] = ahead
        if step < n // 2:
            behind = lax.ppermute(behind, "col", [(i, (i - 1) % n) for i in range(n)])
            got[step] = behind
    return jnp.concatenate([got[k] for k in range(-(n // 2), n - n // 2)], axis=1)


def row_sum(x):
    n = lax.axis_size("row")
    rows, cols = x.shape
    parts = x.reshape(n, rows // n, cols)
    mine = lax.all_to_all(parts, "row", 0, 0, tiled=False).sum(0)
    copies = jnp.broadcast_to(mine[None], (n, rows // n, cols))
    return lax.all_to_all(copies, "row", 0, 0, tiled=False).reshape(rows, cols)


def per_device(panel, slab):
    highest = lax.Precision.HIGHEST
    gathered = col_gather(panel)
    shift = (lax.axis_index("col") - lax.axis_size("col") // 2) * panel.shape[1]
    cross_local = lax.dot_general(gathered, slab, contract_rows, precision=highest)
    gram_local = lax.dot_general(gathered, gathered, contract_rows, precision=highest)
    width = gram_local.shape[1]
    summed = jnp.roll(row_sum(jnp.concatenate([gram_local, cross_local], axis=1)), shift, axis=0)
    gram_total, totals = jnp.roll(summed[:, :width], shift, axis=1), summed[:, width:]
    upper_factor, lower_inverse = factor(gram_total)
    projected = jnp.dot(lower_inverse, totals, precision=highest)
    coefficients = lax.dot_general(lower_inverse, projected, contract_rows, precision=highest)
    residual = slab - jnp.dot(gathered, jnp.roll(coefficients, -shift, axis=0), precision=highest)
    col_width = panel.shape[1]
    rows_total = gathered.shape[0] * lax.axis_size("row")
    scaled = upper_factor * (1.0 / math.sqrt(rows_total))
    triangle = lax.dynamic_slice_in_dim(scaled, lax.axis_index("col") * col_width, col_width, 1)
    return (triangle, projected, residual)


def solution(mesh):
    placed = (P("row", "col"), P("row", "col"))
    return jax.shard_map(
        per_device,
        mesh=mesh,
        in_specs=placed,
        out_specs=(P(None, "col"), P(None, "col"), P("row", "col")),
        check_vma=False,
    )
```

```python
import functools
import math

import jax
import jax.numpy as jnp
from jax import lax
from jax.experimental import pallas as pl
from jax.experimental.pallas import tpu as pltpu
from jax.sharding import PartitionSpec as P

contract_rows = (((0,), (0,)), ((), ()))
HIGHEST = lax.Precision.HIGHEST


def factor_kernel(gram_ref, cross_ref, upper_ref, projected_ref, coefficients_ref, work_ref, left_ref,
                  *, rows_total):
    n = gram_ref.shape[0]
    rows = lax.broadcasted_iota(jnp.int32, (n, n), 0)
    cols = lax.broadcasted_iota(jnp.int32, (n, n), 1)
    work_ref[:, :n] = gram_ref[...]
    work_ref[:, n:] = jnp.where(rows == cols, 1.0, 0.0).astype(jnp.float32)
    depth = 16
    sub_col = lax.broadcasted_iota(jnp.int32, (depth, 1), 0)
    half = n // 2

    def phase(first, last, lo, hi):
        width = hi - lo
        lane = lax.broadcasted_iota(jnp.int32, (depth, width), 1) + lo
        sub = lax.broadcasted_iota(jnp.int32, (depth, width), 0)
        key = n - lo

        def block(b, strip):
            base = pl.multiple_of(b * depth, depth)
            cols = [jnp.sum(jnp.where(lane[:, :128] == base + k, strip[:, :128], 0.0),
                            axis=1, keepdims=True) for k in range(depth)]
            factor_cols, inverse_diag = [], []
            for k in range(depth):
                diag = cols[k][k:k + 1, :]
                guess = lax.rsqrt(diag)
                scale = guess * (1.5 - 0.5 * diag * guess * guess)
                column = jnp.where(sub_col >= k, cols[k] * scale, 0.0)
                factor_cols.append(column)
                inverse_diag.append(scale)
                for m in range(k + 1, depth):
                    cols[m] = cols[m] - column * column[m:m + 1, :]
            done_rows = []
            for k in range(depth):
                row = strip[k:k + 1, :]
                for m in range(k):
                    row = row - factor_cols[m][k:k + 1, :] * done_rows[m]
                done_rows.append(row * inverse_diag[k])
            strip = done_rows[0] + jnp.zeros_like(strip)
            for k in range(1, depth):
                strip = jnp.where(sub == k, done_rows[k], strip)
            work_ref[pl.ds(base, depth), lo:hi] = strip
            left = jnp.where(lane[:, :key] > base + depth - 1, strip[:, :key], 0.0)
            left_ref[lo:n, :] = jnp.transpose(left)
            after = pl.multiple_of(jnp.minimum(base + depth, n - depth), depth)
            nearest = left_ref[pl.ds(after, depth), :]
            following = work_ref[pl.ds(after, depth), lo:hi] - jnp.dot(
                nearest, strip, precision=HIGHEST, preferred_element_type=jnp.float32)
            update = jnp.dot(left_ref[lo:n, :], strip, precision=HIGHEST,
                             preferred_element_type=jnp.float32)
            work_ref[lo:n, lo:hi] = work_ref[lo:n, lo:hi] - update
            return following

        start = work_ref[first * depth:(first + 1) * depth, lo:hi]
        lax.fori_loop(first, last, block, start, unroll=True)

    phase(0, half // depth, 0, n + half)
    phase(half // depth, n // depth, half, 2 * n)
    done = work_ref[...]
    upper_ref[...] = jnp.where(cols >= rows, done[:, :n], 0.0) * (1.0 / math.sqrt(rows_total))
    inverse = jnp.where(cols <= rows, done[:, n:], 0.0)
    projected = jnp.dot(inverse, cross_ref[...], precision=HIGHEST,
                        preferred_element_type=jnp.float32)
    projected_ref[...] = projected
    coefficients_ref[...] = lax.dot_general(inverse, projected, contract_rows, precision=HIGHEST,
                                            preferred_element_type=jnp.float32)


def factor(gram, cross, rows_total):
    n = gram.shape[0]
    return pl.pallas_call(
        functools.partial(factor_kernel, rows_total=rows_total),
        out_shape=(jax.ShapeDtypeStruct((n, n), jnp.float32),
                   jax.ShapeDtypeStruct(cross.shape, jnp.float32),
                   jax.ShapeDtypeStruct(cross.shape, jnp.float32)),
        in_specs=[pl.BlockSpec(memory_space=pltpu.VMEM)] * 2,
        out_specs=(pl.BlockSpec(memory_space=pltpu.VMEM),) * 3,
        scratch_shapes=[pltpu.VMEM((n, 2 * n), jnp.float32), pltpu.VMEM((n, 16), jnp.float32)],
    )(gram, cross)

def col_gather(x):
    n = lax.axis_size("col")
    ahead, behind = x, x
    got = {0: x}
    for step in range(1, n // 2 + 1):
        ahead = lax.ppermute(ahead, "col", [(i, (i + 1) % n) for i in range(n)])
        got[-step] = ahead
        if step < n // 2:
            behind = lax.ppermute(behind, "col", [(i, (i - 1) % n) for i in range(n)])
            got[step] = behind
    return jnp.concatenate([got[k] for k in range(-(n // 2), n - n // 2)], axis=1)


def row_sum(x):
    n = lax.axis_size("row")
    rows, cols = x.shape
    parts = x.reshape(n, rows // n, cols)
    mine = lax.all_to_all(parts, "row", 0, 0, tiled=False).sum(0)
    copies = jnp.broadcast_to(mine[None], (n, rows // n, cols))
    return lax.all_to_all(copies, "row", 0, 0, tiled=False).reshape(rows, cols)


def per_device(panel, slab):
    highest = lax.Precision.HIGHEST
    gathered = col_gather(panel)
    shift = (lax.axis_index("col") - lax.axis_size("col") // 2) * panel.shape[1]
    cross_local = lax.dot_general(gathered, slab, contract_rows, precision=highest)
    gram_local = lax.dot_general(gathered, gathered, contract_rows, precision=highest)
    width = gram_local.shape[1]
    summed = jnp.roll(row_sum(jnp.concatenate([gram_local, cross_local], axis=1)), shift, axis=0)
    gram_total, totals = jnp.roll(summed[:, :width], shift, axis=1), summed[:, width:]
    rows_total = gathered.shape[0] * lax.axis_size("row")
    scaled, projected, coefficients = factor(gram_total, totals, rows_total)
    residual = slab - jnp.dot(gathered, jnp.roll(coefficients, -shift, axis=0), precision=highest)
    col_width = panel.shape[1]
    triangle = lax.dynamic_slice_in_dim(scaled, lax.axis_index("col") * col_width, col_width, 1)
    return (triangle, projected, residual)


def solution(mesh):
    placed = (P("row", "col"), P("row", "col"))
    return jax.shard_map(
        per_device,
        mesh=mesh,
        in_specs=placed,
        out_specs=(P(None, "col"), P(None, "col"), P("row", "col")),
        check_vma=False,
    )
```

```python
import functools
import math

import jax
import jax.numpy as jnp
from jax import lax
from jax.experimental import pallas as pl
from jax.experimental.pallas import tpu as pltpu
from jax.sharding import PartitionSpec as P

contract_rows = (((0,), (0,)), ((), ()))
HIGHEST = lax.Precision.HIGHEST


def factor_kernel(gram_ref, cross_ref, lower_ref, projected_ref, coefficients_ref, work_ref, left_ref,
                  *, rows_total):
    n = gram_ref.shape[0]
    rows = lax.broadcasted_iota(jnp.int32, (n, n), 0)
    cols = lax.broadcasted_iota(jnp.int32, (n, n), 1)
    work_ref[:, :n] = gram_ref[...]
    work_ref[:, n:] = jnp.where(rows == cols, 1.0, 0.0).astype(jnp.float32)
    depth = 16
    sub_col = lax.broadcasted_iota(jnp.int32, (depth, 1), 0)
    half = n // 2

    def phase(first, last, lo, hi):
        width = hi - lo
        lane = lax.broadcasted_iota(jnp.int32, (depth, width), 1) + lo
        sub = lax.broadcasted_iota(jnp.int32, (depth, width), 0)
        key = n - lo

        def block(b, strip):
            base = pl.multiple_of(b * depth, depth)
            cols = [jnp.sum(jnp.where(lane[:, :128] == base + k, strip[:, :128], 0.0),
                            axis=1, keepdims=True) for k in range(depth)]
            factor_cols, inverse_diag = [], []
            for k in range(depth):
                diag = cols[k][k:k + 1, :]
                guess = lax.rsqrt(diag)
                scale = guess * (1.5 - 0.5 * diag * guess * guess)
                column = jnp.where(sub_col >= k, cols[k] * scale, 0.0)
                factor_cols.append(column)
                inverse_diag.append(scale)
                for m in range(k + 1, depth):
                    cols[m] = cols[m] - column * column[m:m + 1, :]
            done_rows = []
            for k in range(depth):
                row = strip[k:k + 1, :]
                for m in range(k):
                    row = row - factor_cols[m][k:k + 1, :] * done_rows[m]
                done_rows.append(row * inverse_diag[k])
            strip = done_rows[0] + jnp.zeros_like(strip)
            for k in range(1, depth):
                strip = jnp.where(sub == k, done_rows[k], strip)
            work_ref[pl.ds(base, depth), lo:hi] = strip
            left = jnp.where(lane[:, :key] > base + depth - 1, strip[:, :key], 0.0)
            left_ref[lo:n, :] = jnp.transpose(left)
            after = pl.multiple_of(jnp.minimum(base + depth, n - depth), depth)
            nearest = left_ref[pl.ds(after, depth), :]
            following = work_ref[pl.ds(after, depth), lo:hi] - jnp.dot(
                nearest, strip, precision=HIGHEST, preferred_element_type=jnp.float32)
            update = jnp.dot(left_ref[lo:n, :], strip, precision=HIGHEST,
                             preferred_element_type=jnp.float32)
            work_ref[lo:n, lo:hi] = work_ref[lo:n, lo:hi] - update
            return following

        start = work_ref[first * depth:(first + 1) * depth, lo:hi]
        lax.fori_loop(first, last, block, start, unroll=True)

    phase(0, half // depth, 0, n + half)
    phase(half // depth, n // depth, half, 2 * n)
    done = work_ref[...]
    lower_ref[...] = jnp.transpose(
        jnp.where(cols >= rows, done[:, :n], 0.0) * (1.0 / math.sqrt(rows_total)))
    inverse = jnp.where(cols <= rows, done[:, n:], 0.0)
    projected = jnp.dot(inverse, cross_ref[...], precision=HIGHEST,
                        preferred_element_type=jnp.float32)
    projected_ref[...] = projected
    coefficients_ref[...] = lax.dot_general(inverse, projected, contract_rows, precision=HIGHEST,
                                            preferred_element_type=jnp.float32)


def factor(gram, cross, rows_total):
    n = gram.shape[0]
    return pl.pallas_call(
        functools.partial(factor_kernel, rows_total=rows_total),
        out_shape=(jax.ShapeDtypeStruct((n, n), jnp.float32),
                   jax.ShapeDtypeStruct(cross.shape, jnp.float32),
                   jax.ShapeDtypeStruct(cross.shape, jnp.float32)),
        in_specs=[pl.BlockSpec(memory_space=pltpu.VMEM)] * 2,
        out_specs=(pl.BlockSpec(memory_space=pltpu.VMEM),) * 3,
        scratch_shapes=[pltpu.VMEM((n, 2 * n), jnp.float32), pltpu.VMEM((n, 16), jnp.float32)],
    )(gram, cross)

def col_gather(x):
    n = lax.axis_size("col")
    ahead, behind = x, x
    got = {0: x}
    for step in range(1, n // 2 + 1):
        ahead = lax.ppermute(ahead, "col", [(i, (i + 1) % n) for i in range(n)])
        got[-step] = ahead
        if step < n // 2:
            behind = lax.ppermute(behind, "col", [(i, (i - 1) % n) for i in range(n)])
            got[step] = behind
    return jnp.concatenate([got[k] for k in range(-(n // 2), n - n // 2)], axis=1)


def row_sum(x):
    n = lax.axis_size("row")
    rows, cols = x.shape
    parts = x.reshape(n, rows // n, cols)
    mine = lax.all_to_all(parts, "row", 0, 0, tiled=False).sum(0)
    copies = jnp.broadcast_to(mine[None], (n, rows // n, cols))
    return lax.all_to_all(copies, "row", 0, 0, tiled=False).reshape(rows, cols)


def per_device(panel, slab):
    highest = lax.Precision.HIGHEST
    gathered = col_gather(panel)
    shift = (lax.axis_index("col") - lax.axis_size("col") // 2) * panel.shape[1]
    cross_local = lax.dot_general(gathered, slab, contract_rows, precision=highest)
    gram_local = lax.dot_general(gathered, gathered, contract_rows, precision=highest)
    width = gram_local.shape[1]
    summed = jnp.roll(row_sum(jnp.concatenate([gram_local, cross_local], axis=1)), shift, axis=0)
    gram_total, totals = jnp.roll(summed[:, :width], shift, axis=1), summed[:, width:]
    rows_total = gathered.shape[0] * lax.axis_size("row")
    scaled, projected, coefficients = factor(gram_total, totals, rows_total)
    residual = slab - jnp.dot(gathered, jnp.roll(coefficients, -shift, axis=0), precision=highest)
    col_width = panel.shape[1]
    triangle = lax.dynamic_slice_in_dim(scaled, lax.axis_index("col") * col_width, col_width, 0).T
    return (triangle, projected, residual)


def solution(mesh):
    placed = (P("row", "col"), P("row", "col"))
    return jax.shard_map(
        per_device,
        mesh=mesh,
        in_specs=placed,
        out_specs=(P(None, "col"), P(None, "col"), P("row", "col")),
        check_vma=False,
    )
```
